512 devices in a mesh: wide: 64 (over y, z), narrow: 8 (over x, core).
Axes of the slice: x: 4, y: 8, z: 8, core: 2. Of those that a mesh axis runs over, the one named last changes fastest.
Arguments:
- amplitudes: bfloat16 [384, 2048], P('wide', 'narrow'), may hold values from -6 to 6
- integrals: bfloat16 [262144, 2048], P('wide', 'narrow'), may hold values from -0.375 to 0.375
- virtual_irrep: int32 [512], replicated, may hold values from 0 to 7
- column_irrep: int32 [2048], P('narrow'), may hold values from 0 to 7
- pair_energy: float32 [384], P('narrow'), may hold values from -4 to -1
- virtual_energy: float32 [512], replicated, may hold values from 0.5 to 3
- residual_in: bfloat16 [384, 262144], P('narrow', 'wide'), may hold values from -6 to 6
Outputs:
- new_amplitudes: bfloat16 [384, 262144], P('narrow', 'wide')
The draws below stay inside these ranges and needn't reach their ends.
All inputs are finite; a program needn't handle non-finite values.
Results may differ from the reference program's by a relative error of at most 0.012.
Values may be sent and summed in bfloat16 or wider, within the bound.
No kernel may reach another device: no remote copies, remote signals or barrier semaphores. Data moves between devices by JAX's collectives and lax.ppermute only.
A program may use at most 64 MiB of HBM per device.

```python
import jax
import jax.numpy as jnp
from jax import lax

NV = 512
NIRREP = 8
CD_DEV = 256
OO = 384
AB = 262144
CD = 2048
N_NARROW = 8


def with_ends(array, rng, smallest, high):
    longest = array.shape.index(max(array.shape))
    spots = []
    for shift in (0, 1):
        where = [jax.random.randint(jax.random.fold_in(rng, axis), (), 0, length) for axis, length in enumerate(array.shape)]
        where[longest] = (where[longest] + shift) % array.shape[longest]
        spots.append(tuple(where))
    return array.at[spots[0]].set(smallest).at[spots[1]].set(high)


def shard_levels(key, shape, cuts, smallest, largest):
    loudness = 1.0
    for position, blocks in cuts:
        draws = jax.random.uniform(jax.random.fold_in(jax.random.fold_in(key, 6), position), (blocks,), jnp.float32, smallest / len(cuts), largest / len(cuts))
        loudness = loudness * jnp.repeat(jnp.exp(draws), shape[position] // blocks).reshape((-1,) + (1,) * (len(shape) - 1 - position))
    return loudness


def bell_draw(rng, extent, deviation, most, split=(), kind=jnp.bfloat16):
    result = deviation * jax.random.normal(rng, extent, jnp.float32)
    if split:
        result = result * shard_levels(rng, extent, split, -0.22, 0.18)
    return jnp.clip(result, -most, most).astype(kind)


def setup_inputs(seed: int = 0) -> dict:
    arg_keys = jax.random.split(jax.random.key(seed), 8)
    amplitudes = bell_draw(arg_keys[0], (OO, CD), 1.0, 6.0, ((0, 64), (1, 8)))
    integrals = bell_draw(arg_keys[1], (AB, CD), (CD // 8) ** -0.5, 0.375, ((0, 64), (1, 8)))
    virtual_irrep = with_ends(jax.random.randint(arg_keys[2], (NV,), 0, NIRREP), jax.random.fold_in(arg_keys[2], 1), 0, NIRREP - 1).astype(jnp.int32)
    column_irrep = with_ends(jax.random.randint(arg_keys[3], (CD,), 0, NIRREP), jax.random.fold_in(arg_keys[3], 1), 0, NIRREP - 1).astype(jnp.int32)
    pair_energy = jnp.clip(-4.0 + 3.0 * jax.random.uniform(arg_keys[4], (OO,), jnp.float32) ** shard_levels(arg_keys[4], (OO,), ((0, 8),), -0.2, 0.2), -4.0, -1.0)
    virtual_energy = jnp.clip(jax.random.uniform(arg_keys[5], (NV,), jnp.float32, 0.5, 3.0), 0.5, 3.0)
    residual_in = bell_draw(arg_keys[6], (OO, AB), 1.0, 6.0, ((0, 8), (1, 64)))
    return {"amplitudes": amplitudes, "integrals": integrals, "virtual_irrep": virtual_irrep, "column_irrep": column_irrep, "pair_energy": pair_energy, "virtual_energy": virtual_energy, "residual_in": residual_in}


def reference(amplitudes, integrals, virtual_irrep, column_irrep, pair_energy, virtual_energy, residual_in):
    amp_wide = amplitudes.astype(jnp.float32).reshape(OO, N_NARROW, CD_DEV)
    row_irrep = jnp.bitwise_xor(virtual_irrep[:, None], virtual_irrep[None, :]).reshape(NV * NV)
    block_size = 8 * NV
    block_count = NV // 8

    def block_ladder(index):
        offset = (index * block_size).astype(jnp.int32)
        rows_block = lax.dynamic_slice_in_dim(integrals, offset, block_size, 0)
        irrep_block = lax.dynamic_slice_in_dim(row_irrep, offset, block_size, 0)
        masked = jnp.where(irrep_block[:, None] == column_irrep[None, :], rows_block, jnp.zeros((), jnp.bfloat16))
        masked_wide = masked.astype(jnp.float32).reshape(block_size, N_NARROW, CD_DEV)
        partial_value = jnp.einsum('ogc,bgc->gob', amp_wide, masked_wide)
        rounded = lax.optimization_barrier(partial_value.astype(jnp.bfloat16))
        return jnp.sum(rounded.astype(jnp.float32), axis=0)

    ladder = lax.map(block_ladder, jnp.arange(block_count, dtype=jnp.int32))
    ladder = jnp.transpose(ladder, (1, 0, 2)).reshape(OO, NV, NV)
    mirrored = jnp.transpose(ladder, (0, 2, 1))
    denominator = pair_energy[:, None, None] - virtual_energy[None, :, None] - virtual_energy[None, None, :]
    total = residual_in.astype(jnp.float32).reshape(OO, NV, NV) + ladder - mirrored
    return (total / denominator).reshape(OO, NV * NV).astype(jnp.bfloat16)
```

```python
import jax
import jax.numpy as jnp
from jax import lax
from jax.sharding import Mesh
from jax.sharding import PartitionSpec as P

WIDE = ("y", "z")
NARROW = ("x", "c")


def local(
    amplitudes, integrals, virtual_irrep, column_irrep, pair_energy, virtual_energy, residual_in
):
    ny, nz = lax.axis_size("y"), lax.axis_size("z")
    nx, nc = lax.axis_size("x"), lax.axis_size("c")
    wide_size = ny * nz
    num_virt = virtual_irrep.shape[0]
    a_local = num_virt // wide_size
    wide_index = lax.axis_index("y") * nz + lax.axis_index("z")
    first_a = wide_index * a_local
    local_irrep = lax.dynamic_slice_in_dim(virtual_irrep, first_a, a_local, 0)
    row_irrep = jnp.bitwise_xor(local_irrep[:, None], virtual_irrep[None, :]).reshape(
        a_local * num_virt
    )
    masked = jnp.where(
        row_irrep[:, None] == column_irrep[None, :], integrals, jnp.zeros((), integrals.dtype)
    )
    amp = lax.all_gather(amplitudes, "z", axis=0, tiled=True)
    amp = lax.all_gather(amp, "y", axis=0, tiled=True)
    pairs = amp.shape[0]
    block = pairs // (nx * nc)
    amp = amp.reshape(nx, nc, block, amp.shape[1]).transpose(1, 0, 2, 3).reshape(pairs, -1)
    contract = (((1,), (1,)), ((), ()))
    terms = lax.dot_general(amp, masked, contract, preferred_element_type=jnp.float32)
    terms = terms.astype(jnp.bfloat16)
    terms = lax.psum_scatter(terms, "c", scatter_dimension=0, tiled=True)
    ladder = lax.psum_scatter(terms, "x", scatter_dimension=0, tiled=True).astype(jnp.float32)
    pair_rows = ladder.shape[0]
    ladder_cube = ladder.reshape(pair_rows, a_local, num_virt)
    swapped = lax.all_to_all(
        ladder_cube.astype(jnp.bfloat16), WIDE, split_axis=2, concat_axis=2, tiled=True
    ).astype(ladder_cube.dtype)
    mirrored = swapped.reshape(pair_rows, a_local, wide_size, a_local)
    mirrored = jnp.transpose(mirrored, (0, 3, 2, 1)).reshape(pair_rows, a_local * num_virt)
    local_energy = lax.dynamic_slice_in_dim(virtual_energy, first_a, a_local, 0)
    denominator = (
        pair_energy[:, None, None] - local_energy[None, :, None] - virtual_energy[None, None, :]
    )
    denominator = denominator.reshape(pair_rows, a_local * num_virt)
    total = residual_in.astype(jnp.float32) + ladder - mirrored
    return (total / denominator).astype(jnp.bfloat16)


def solution(mesh):
    ny, nz = 8, mesh.devices.shape[0] // 8
    nx, nc = mesh.devices.shape[1] // 2, 2
    fine = Mesh(mesh.devices.reshape(ny, nz, nx, nc), ("y", "z", "x", "c"))
    return jax.shard_map(
        local,
        mesh=fine,
        in_specs=(
            P(WIDE, NARROW),
            P(WIDE, NARROW),
            P(),
            P(NARROW),
            P(NARROW),
            P(),
            P(NARROW, WIDE),
        ),
        out_specs=P(NARROW, WIDE),
        check_vma=False,
    )
```

```python
import jax
import jax.numpy as jnp
from jax import lax
from jax.sharding import Mesh
from jax.sharding import PartitionSpec as P

WIDE = ("y", "z")
NARROW = ("x", "c")


def gather_rows(block, name):
    n = lax.axis_size(name)
    copies = jnp.broadcast_to(block[None], (n,) + block.shape)
    got = lax.all_to_all(copies, name, 0, 0, tiled=True)
    return got.reshape((n * block.shape[0],) + block.shape[1:])


def local(
    amplitudes, integrals, virtual_irrep, column_irrep, pair_energy, virtual_energy, residual_in
):
    nz = lax.axis_size("z")
    wide_size = lax.axis_size("y") * nz
    num_virt = virtual_irrep.shape[0]
    a_local = num_virt // wide_size
    wide_index = lax.axis_index("y") * nz + lax.axis_index("z")
    first_a = wide_index * a_local
    local_irrep = lax.dynamic_slice_in_dim(virtual_irrep, first_a, a_local, 0)
    row_irrep = jnp.bitwise_xor(local_irrep[:, None], virtual_irrep[None, :]).reshape(
        a_local * num_virt
    )
    masked = jnp.where(
        row_irrep[:, None] == column_irrep[None, :], integrals, jnp.zeros((), integrals.dtype)
    )
    amp = gather_rows(gather_rows(amplitudes, "z"), "y")
    contract = (((1,), (1,)), ((), ()))
    terms = lax.dot_general(amp, masked, contract, preferred_element_type=jnp.float32)
    ladder = lax.psum_scatter(
        terms.astype(jnp.bfloat16), NARROW, scatter_dimension=0, tiled=True
    ).astype(jnp.float32)
    pair_rows = ladder.shape[0]
    outgoing = ladder.astype(jnp.bfloat16).reshape(pair_rows, a_local, wide_size, a_local)
    outgoing = jnp.transpose(outgoing, (2, 0, 1, 3))
    got = lax.all_to_all(outgoing, WIDE, 0, 0, tiled=True)
    mirrored = jnp.transpose(got, (1, 3, 0, 2)).astype(jnp.float32)
    mirrored = mirrored.reshape(pair_rows, a_local * num_virt)
    local_energy = lax.dynamic_slice_in_dim(virtual_energy, first_a, a_local, 0)
    denominator = (
        pair_energy[:, None, None] - local_energy[None, :, None] - virtual_energy[None, None, :]
    )
    denominator = denominator.reshape(pair_rows, a_local * num_virt)
    total = residual_in.astype(jnp.float32) + ladder - mirrored
    return (total / denominator).astype(jnp.bfloat16)


def solution(mesh):
    wide, narrow = mesh.devices.shape
    fine = Mesh(mesh.devices.reshape(8, wide // 8, narrow // 2, 2), ("y", "z", "x", "c"))
    return jax.shard_map(
        local,
        mesh=fine,
        in_specs=(
            P(WIDE, NARROW),
            P(WIDE, NARROW),
            P(),
            P(NARROW),
            P(NARROW),
            P(),
            P(NARROW, WIDE),
        ),
        out_specs=P(NARROW, WIDE),
        check_vma=False,
    )
```

```python
import jax
import jax.numpy as jnp
from jax import lax
from jax.sharding import Mesh
from jax.sharding import PartitionSpec as P

WIDE = ("y", "z")
NARROW = ("x", "c")


def gather_rows(block, name):
    n = lax.axis_size(name)
    copies = jnp.broadcast_to(block[None], (n,) + block.shape)
    got = lax.all_to_all(copies, name, 0, 0, tiled=True)
    return got.reshape((n * block.shape[0],) + block.shape[1:])


def local(
    amplitudes, integrals, virtual_irrep, column_irrep, pair_energy, virtual_energy, residual_in
):
    nz = lax.axis_size("z")
    wide_size = lax.axis_size("y") * nz
    num_virt = virtual_irrep.shape[0]
    a_local = num_virt // wide_size
    cd_local = integrals.shape[1]
    wide_index = lax.axis_index("y") * nz + lax.axis_index("z")
    first_a = wide_index * a_local
    outgoing = integrals.reshape(a_local, wide_size, a_local, cd_local).transpose(1, 0, 2, 3)
    got = lax.all_to_all(outgoing, WIDE, 0, 0, tiled=True)
    swapped = got.transpose(2, 0, 1, 3).reshape(a_local * num_virt, cd_local)
    local_irrep = lax.dynamic_slice_in_dim(virtual_irrep, first_a, a_local, 0)
    row_irrep = jnp.bitwise_xor(local_irrep[:, None], virtual_irrep[None, :]).reshape(
        a_local * num_virt
    )
    keep = row_irrep[:, None] == column_irrep[None, :]
    zero = jnp.zeros((), integrals.dtype)
    masked = jnp.where(keep, integrals, zero)
    masked_swapped = jnp.where(keep, swapped, zero)
    amp = gather_rows(gather_rows(amplitudes, "z"), "y")
    contract = (((1,), (1,)), ((), ()))
    direct = lax.dot_general(amp, masked, contract, preferred_element_type=jnp.float32)
    mirror = lax.dot_general(amp, masked_swapped, contract, preferred_element_type=jnp.float32)
    diff = direct.astype(jnp.bfloat16).astype(jnp.float32) - mirror.astype(
        jnp.bfloat16
    ).astype(jnp.float32)
    ladder = lax.psum_scatter(
        diff.astype(jnp.bfloat16), NARROW, scatter_dimension=0, tiled=True
    ).astype(jnp.float32)
    pair_rows = ladder.shape[0]
    local_energy = lax.dynamic_slice_in_dim(virtual_energy, first_a, a_local, 0)
    denominator = (
        pair_energy[:, None, None] - local_energy[None, :, None] - virtual_energy[None, None, :]
    )
    denominator = denominator.reshape(pair_rows, a_local * num_virt)
    total = residual_in.astype(jnp.float32) + ladder
    return (total / denominator).astype(jnp.bfloat16)


def solution(mesh):
    wide, narrow = mesh.devices.shape
    fine = Mesh(mesh.devices.reshape(8, wide // 8, narrow // 2, 2), ("y", "z", "x", "c"))
    return jax.shard_map(
        local,
        mesh=fine,
        in_specs=(
            P(WIDE, NARROW),
            P(WIDE, NARROW),
            P(),
            P(NARROW),
            P(NARROW),
            P(),
            P(NARROW, WIDE),
        ),
        out_specs=P(NARROW, WIDE),
        check_vma=False,
    )
```

```python
import jax
import jax.numpy as jnp
from jax import lax
from jax.sharding import Mesh
from jax.sharding import PartitionSpec as P

WIDE = ("y", "z")
NARROW = ("x", "c")


def gather_rows(block, name):
    n = lax.axis_size(name)
    copies = jnp.broadcast_to(block[None], (n,) + block.shape)
    got = lax.all_to_all(copies, name, 0, 0, tiled=True)
    return got.reshape((n * block.shape[0],) + block.shape[1:])


def local(
    amplitudes, integrals, virtual_irrep, column_irrep, pair_energy, virtual_energy, residual_in
):
    nz = lax.axis_size("z")
    wide_size = lax.axis_size("y") * nz
    num_virt = virtual_irrep.shape[0]
    a_local = num_virt // wide_size
    wide_index = lax.axis_index("y") * nz + lax.axis_index("z")
    first_a = wide_index * a_local
    local_irrep = lax.dynamic_slice_in_dim(virtual_irrep, first_a, a_local, 0)
    row_irrep = jnp.bitwise_xor(local_irrep[:, None], virtual_irrep[None, :]).reshape(
        a_local * num_virt
    )
    masked = jnp.where(
        row_irrep[:, None] == column_irrep[None, :], integrals, jnp.zeros((), integrals.dtype)
    )
    amp = gather_rows(gather_rows(amplitudes, "z"), "y")
    contract = (((1,), (1,)), ((), ()))
    terms = lax.dot_general(amp, masked, contract, preferred_element_type=jnp.float32)
    nx, nc = lax.axis_size("x"), lax.axis_size("c")
    block = terms.shape[0] // (nx * nc)
    parts = terms.astype(jnp.bfloat16).reshape(nx, nc, block, terms.shape[1])
    parts = lax.all_to_all(parts, "c", 1, 1, tiled=True)
    parts = parts.astype(jnp.float32).sum(axis=1).astype(jnp.bfloat16)
    parts = lax.all_to_all(parts, "x", 0, 0, tiled=True)
    ladder = parts.astype(jnp.float32).sum(axis=0)
    pair_rows = ladder.shape[0]
    outgoing = ladder.astype(jnp.bfloat16).reshape(pair_rows, a_local, wide_size, a_local)
    outgoing = jnp.transpose(outgoing, (2, 0, 1, 3))
    got = lax.all_to_all(outgoing, WIDE, 0, 0, tiled=True)
    mirrored = jnp.transpose(got, (1, 3, 0, 2)).astype(jnp.float32)
    mirrored = mirrored.reshape(pair_rows, a_local * num_virt)
    local_energy = lax.dynamic_slice_in_dim(virtual_energy, first_a, a_local, 0)
    denominator = (
        pair_energy[:, None, None] - local_energy[None, :, None] - virtual_energy[None, None, :]
    )
    denominator = denominator.reshape(pair_rows, a_local * num_virt)
    total = residual_in.astype(jnp.float32) + ladder - mirrored
    return (total / denominator).astype(jnp.bfloat16)


def solution(mesh):
    wide, narrow = mesh.devices.shape
    fine = Mesh(mesh.devices.reshape(8, wide // 8, narrow // 2, 2), ("y", "z", "x", "c"))
    return jax.shard_map(
        local,
        mesh=fine,
        in_specs=(
            P(WIDE, NARROW),
            P(WIDE, NARROW),
            P(),
            P(NARROW),
            P(NARROW),
            P(),
            P(NARROW, WIDE),
        ),
        out_specs=P(NARROW, WIDE),
        check_vma=False,
    )
```

```python
import jax
import jax.numpy as jnp
from jax import lax
from jax.sharding import Mesh
from jax.sharding import PartitionSpec as P

WIDE = ("y", "z")
NARROW = ("x", "c")


def gather_rows(block, name, n):
    copies = jnp.broadcast_to(block[None], (n,) + block.shape)
    return lax.all_to_all(copies, name, 0, 0, tiled=True)


def local(
    amplitudes, integrals, virtual_irrep, column_irrep, pair_energy, virtual_energy, residual_in
):
    ny, nz = lax.axis_size("y"), lax.axis_size("z")
    nx, nc = lax.axis_size("x"), lax.axis_size("c")
    wide_size = ny * nz
    num_virt = virtual_irrep.shape[0]
    a_local = num_virt // wide_size
    cd_local = integrals.shape[1]
    core = lax.axis_index("c")
    wide_index = lax.axis_index("y") * nz + lax.axis_index("z")
    first_a = wide_index * a_local
    swap = [(0, 1), (1, 0)]
    partner_integrals = lax.ppermute(integrals, "c", swap)
    partner_irrep = lax.ppermute(column_irrep, "c", swap)
    local_irrep = lax.dynamic_slice_in_dim(virtual_irrep, first_a, a_local, 0)
    row_irrep = jnp.bitwise_xor(local_irrep[:, None], virtual_irrep[None, :]).reshape(
        a_local * num_virt
    )
    zero = jnp.zeros((), integrals.dtype)
    masked = jnp.where(row_irrep[:, None] == column_irrep[None, :], integrals, zero)
    masked_partner = jnp.where(
        row_irrep[:, None] == partner_irrep[None, :], partner_integrals, zero
    )
    amp = gather_rows(amplitudes, ("z", "c"), nz * nc)
    amp = gather_rows(amp, "y", ny)
    rows = amplitudes.shape[0]
    amp = amp.reshape(ny // nc, nc, nz, nc, rows, cd_local)
    amp = lax.dynamic_index_in_dim(amp, core, 1, keepdims=False)
    own = lax.dynamic_index_in_dim(amp, core, 2, keepdims=False)
    other = lax.dynamic_index_in_dim(amp, 1 - core, 2, keepdims=False)
    pairs = own.shape[0] * own.shape[1] * own.shape[2]
    own = own.reshape(pairs, cd_local)
    other = other.reshape(pairs, cd_local)
    contract = (((1,), (1,)), ((), ()))
    part_own = lax.dot_general(own, masked, contract, preferred_element_type=jnp.float32)
    part_other = lax.dot_general(
        other, masked_partner, contract, preferred_element_type=jnp.float32
    )
    pair_sum = part_own.astype(jnp.bfloat16).astype(jnp.float32) + part_other.astype(
        jnp.bfloat16
    ).astype(jnp.float32)
    block = pairs // nx
    parts = pair_sum.astype(jnp.bfloat16).reshape(nx, block, pair_sum.shape[1])
    parts = lax.all_to_all(parts, "x", 0, 0, tiled=True)
    ladder = parts.astype(jnp.float32).sum(axis=0)
    pair_rows = ladder.shape[0]
    outgoing = ladder.astype(jnp.bfloat16).reshape(pair_rows, a_local, wide_size, a_local)
    outgoing = jnp.transpose(outgoing, (2, 0, 1, 3))
    got = lax.all_to_all(outgoing, WIDE, 0, 0, tiled=True)
    mirrored = jnp.transpose(got, (1, 3, 0, 2)).astype(jnp.float32)
    mirrored = mirrored.reshape(pair_rows, a_local * num_virt)
    local_energy = lax.dynamic_slice_in_dim(virtual_energy, first_a, a_local, 0)
    denominator = (
        pair_energy[:, None, None] - local_energy[None, :, None] - virtual_energy[None, None, :]
    )
    denominator = denominator.reshape(pair_rows, a_local * num_virt)
    total = residual_in.astype(jnp.float32) + ladder - mirrored
    return (total / denominator).astype(jnp.bfloat16)


def solution(mesh):
    wide, narrow = mesh.devices.shape
    fine = Mesh(mesh.devices.reshape(8, wide // 8, narrow // 2, 2), ("y", "z", "x", "c"))
    return jax.shard_map(
        local,
        mesh=fine,
        in_specs=(
            P(WIDE, NARROW),
            P(WIDE, NARROW),
            P(),
            P(NARROW),
            P(NARROW),
            P(),
            P(NARROW, WIDE),
        ),
        out_specs=P(NARROW, WIDE),
        check_vma=False,
    )
```

```python
import jax
import jax.numpy as jnp
from jax import lax
from jax.sharding import Mesh
from jax.sharding import PartitionSpec as P

WIDE = ("y", "z")
NARROW = ("x", "c")


def gather_rows(block, name):
    n = lax.axis_size(name) if isinstance(name, str) else lax.axis_size(name[0]) * lax.axis_size(name[1])
    copies = jnp.broadcast_to(block[None], (n,) + block.shape)
    got = lax.all_to_all(copies, name, 0, 0, tiled=True)
    return got.reshape((n * block.shape[0],) + block.shape[1:])


def local(
    amplitudes, integrals, virtual_irrep, column_irrep, pair_energy, virtual_energy, residual_in
):
    nz = lax.axis_size("z")
    wide_size = lax.axis_size("y") * nz
    num_virt = virtual_irrep.shape[0]
    a_local = num_virt // wide_size
    wide_index = lax.axis_index("y") * nz + lax.axis_index("z")
    first_a = wide_index * a_local
    local_irrep = lax.dynamic_slice_in_dim(virtual_irrep, first_a, a_local, 0)
    row_irrep = jnp.bitwise_xor(local_irrep[:, None], virtual_irrep[None, :]).reshape(
        a_local * num_virt
    )
    masked = jnp.where(
        row_irrep[:, None] == column_irrep[None, :], integrals, jnp.zeros((), integrals.dtype)
    )
    amp = gather_rows(amplitudes, WIDE)
    contract = (((1,), (1,)), ((), ()))
    terms = lax.dot_general(amp, masked, contract, preferred_element_type=jnp.float32)
    nx, nc = lax.axis_size("x"), lax.axis_size("c")
    block = terms.shape[0] // (nx * nc)
    parts = terms.astype(jnp.bfloat16).reshape(nx, nc, block, terms.shape[1])
    parts = lax.all_to_all(parts, "c", 1, 1, tiled=True)
    parts = parts.astype(jnp.float32).sum(axis=1).astype(jnp.bfloat16)
    parts = lax.all_to_all(parts, "x", 0, 0, tiled=True)
    ladder = parts.astype(jnp.float32).sum(axis=0)
    pair_rows = ladder.shape[0]
    outgoing = ladder.astype(jnp.bfloat16).reshape(pair_rows, a_local, wide_size, a_local)
    outgoing = jnp.transpose(outgoing, (2, 0, 1, 3)).reshape(wide_size, -1, 128)
    got = lax.all_to_all(outgoing, WIDE, 0, 0, tiled=True)
    got = got.reshape(wide_size, pair_rows, a_local, a_local)
    mirrored = jnp.transpose(got, (1, 3, 0, 2)).astype(jnp.float32)
    mirrored = mirrored.reshape(pair_rows, a_local * num_virt)
    local_energy = lax.dynamic_slice_in_dim(virtual_energy, first_a, a_local, 0)
    denominator = (
        pair_energy[:, None, None] - local_energy[None, :, None] - virtual_energy[None, None, :]
    )
    denominator = denominator.reshape(pair_rows, a_local * num_virt)
    total = residual_in.astype(jnp.float32) + ladder - mirrored
    return (total / denominator).astype(jnp.bfloat16)


def solution(mesh):
    wide, narrow = mesh.devices.shape
    fine = Mesh(mesh.devices.reshape(8, wide // 8, narrow // 2, 2), ("y", "z", "x", "c"))
    return jax.shard_map(
        local,
        mesh=fine,
        in_specs=(
            P(WIDE, NARROW),
            P(WIDE, NARROW),
            P(),
            P(NARROW),
            P(NARROW),
            P(),
            P(NARROW, WIDE),
        ),
        out_specs=P(NARROW, WIDE),
        check_vma=False,
    )
```

```python
import jax
import jax.numpy as jnp
from jax import lax
from jax.sharding import Mesh
from jax.sharding import PartitionSpec as P

WIDE = ("y", "z")
NARROW = ("x", "c")


def gather_rows(block, name):
    n = 1
    for axis in name:
        n *= lax.axis_size(axis)
    copies = jnp.broadcast_to(block[None], (n,) + block.shape)
    got = lax.all_to_all(copies, name, 0, 0, tiled=True)
    return got.reshape((n * block.shape[0],) + block.shape[1:])


def local(
    amplitudes, integrals, virtual_irrep, column_irrep, pair_energy, virtual_energy, residual_in
):
    nz = lax.axis_size("z")
    wide_size = lax.axis_size("y") * nz
    num_virt = virtual_irrep.shape[0]
    a_local = num_virt // wide_size
    wide_index = lax.axis_index("y") * nz + lax.axis_index("z")
    first_a = wide_index * a_local
    local_irrep = lax.dynamic_slice_in_dim(virtual_irrep, first_a, a_local, 0)
    row_irrep = jnp.bitwise_xor(local_irrep[:, None], virtual_irrep[None, :]).reshape(
        a_local * num_virt
    )
    masked = jnp.where(
        row_irrep[:, None] == column_irrep[None, :], integrals, jnp.zeros((), integrals.dtype)
    )
    amp = gather_rows(amplitudes, WIDE)
    contract = (((1,), (1,)), ((), ()))
    terms = lax.dot_general(amp, masked, contract, preferred_element_type=jnp.float32)
    nx, nc = lax.axis_size("x"), lax.axis_size("c")
    block = terms.shape[0] // (nx * nc)
    parts = terms.astype(jnp.bfloat16).reshape(nx, nc, block, terms.shape[1])
    parts = lax.all_to_all(parts, "c", 1, 1, tiled=True)
    parts = parts.astype(jnp.float32).sum(axis=1).astype(jnp.bfloat16)
    parts = lax.all_to_all(parts, "x", 0, 0, tiled=True)
    ladder = parts.astype(jnp.float32).sum(axis=0)
    pair_rows = ladder.shape[0]
    outgoing = ladder.astype(jnp.bfloat16).reshape(pair_rows, a_local, wide_size, a_local)
    outgoing = jnp.transpose(outgoing, (2, 0, 1, 3))
    got = lax.all_to_all(outgoing, WIDE, 0, 0, tiled=True)
    mirrored = jnp.transpose(got, (1, 3, 0, 2)).astype(jnp.float32)
    mirrored = mirrored.reshape(pair_rows, a_local * num_virt)
    local_energy = lax.dynamic_slice_in_dim(virtual_energy, first_a, a_local, 0)
    denominator = (
        pair_energy[:, None, None] - local_energy[None, :, None] - virtual_energy[None, None, :]
    )
    denominator = denominator.reshape(pair_rows, a_local * num_virt)
    total = residual_in.astype(jnp.float32) + ladder - mirrored
    return (total / denominator).astype(jnp.bfloat16)


def solution(mesh):
    wide, narrow = mesh.devices.shape
    fine = Mesh(mesh.devices.reshape(8, wide // 8, narrow // 2, 2), ("y", "z", "x", "c"))
    return jax.shard_map(
        local,
        mesh=fine,
        in_specs=(
            P(WIDE, NARROW),
            P(WIDE, NARROW),
            P(),
            P(NARROW),
            P(NARROW),
            P(),
            P(NARROW, WIDE),
        ),
        out_specs=P(NARROW, WIDE),
        check_vma=False,
    )
```

```python
import jax
import jax.numpy as jnp
from jax import lax
from jax.sharding import Mesh
from jax.sharding import PartitionSpec as P

WIDE = ("y", "z")
NARROW = ("x", "c")


def gather_rows(block, name):
    n = 1
    for axis in name:
        n *= lax.axis_size(axis)
    copies = jnp.broadcast_to(block[None], (n,) + block.shape)
    got = lax.all_to_all(copies, name, 0, 0, tiled=True)
    return got.reshape((n * block.shape[0],) + block.shape[1:])


def local(
    amplitudes, integrals, virtual_irrep, column_irrep, pair_energy, virtual_energy, residual_in
):
    nz = lax.axis_size("z")
    wide_size = lax.axis_size("y") * nz
    num_virt = virtual_irrep.shape[0]
    a_local = num_virt // wide_size
    wide_index = lax.axis_index("y") * nz + lax.axis_index("z")
    first_a = wide_index * a_local
    core = lax.axis_index("c")
    nx, nc = lax.axis_size("x"), lax.axis_size("c")
    cd_local = integrals.shape[1]
    swap = [(0, 1), (1, 0)]
    partner_integrals = lax.ppermute(integrals, "c", swap)
    partner_irrep = lax.ppermute(column_irrep, "c", swap)
    local_irrep = lax.dynamic_slice_in_dim(virtual_irrep, first_a, a_local, 0)
    row_irrep = jnp.bitwise_xor(local_irrep[:, None], virtual_irrep[None, :]).reshape(
        a_local * num_virt
    )
    zero = jnp.zeros((), integrals.dtype)
    masked = jnp.where(row_irrep[:, None] == column_irrep[None, :], integrals, zero)
    masked_partner = jnp.where(
        row_irrep[:, None] == partner_irrep[None, :], partner_integrals, zero
    )
    rows = amplitudes.shape[0]
    amp = gather_rows(amplitudes, ("y", "z", "c"))
    amp = amp.reshape(lax.axis_size("y") // nc, nc, nz, nc, rows, cd_local)
    amp = lax.dynamic_index_in_dim(amp, core, 1, keepdims=False)
    own = lax.dynamic_index_in_dim(amp, core, 2, keepdims=False)
    other = lax.dynamic_index_in_dim(amp, 1 - core, 2, keepdims=False)
    pairs = own.shape[0] * own.shape[1] * own.shape[2]
    own = own.reshape(pairs, cd_local)
    other = other.reshape(pairs, cd_local)
    contract = (((1,), (1,)), ((), ()))
    part_own = lax.dot_general(own, masked, contract, preferred_element_type=jnp.float32)
    part_other = lax.dot_general(
        other, masked_partner, contract, preferred_element_type=jnp.float32
    )
    pair_sum = part_own.astype(jnp.bfloat16).astype(jnp.float32) + part_other.astype(
        jnp.bfloat16
    ).astype(jnp.float32)
    parts = pair_sum.astype(jnp.bfloat16).reshape(nx, pairs // nx, pair_sum.shape[1])
    parts = lax.all_to_all(parts, "x", 0, 0, tiled=True)
    ladder = parts.astype(jnp.float32).sum(axis=0)
    pair_rows = ladder.shape[0]
    outgoing = ladder.astype(jnp.bfloat16).reshape(pair_rows, a_local, wide_size, a_local)
    outgoing = jnp.transpose(outgoing, (2, 0, 1, 3))
    got = lax.all_to_all(outgoing, WIDE, 0, 0, tiled=True)
    mirrored = jnp.transpose(got, (1, 3, 0, 2)).astype(jnp.float32)
    mirrored = mirrored.reshape(pair_rows, a_local * num_virt)
    local_energy = lax.dynamic_slice_in_dim(virtual_energy, first_a, a_local, 0)
    denominator = (
        pair_energy[:, None, None] - local_energy[None, :, None] - virtual_energy[None, None, :]
    )
    denominator = denominator.reshape(pair_rows, a_local * num_virt)
    total = residual_in.astype(jnp.float32) + ladder - mirrored
    return (total / denominator).astype(jnp.bfloat16)


def solution(mesh):
    wide, narrow = mesh.devices.shape
    fine = Mesh(mesh.devices.reshape(8, wide // 8, narrow // 2, 2), ("y", "z", "x", "c"))
    return jax.shard_map(
        local,
        mesh=fine,
        in_specs=(
            P(WIDE, NARROW),
            P(WIDE, NARROW),
            P(),
            P(NARROW),
            P(NARROW),
            P(),
            P(NARROW, WIDE),
        ),
        out_specs=P(NARROW, WIDE),
        check_vma=False,
    )
```

```python
import jax
import jax.numpy as jnp
from jax import lax
from jax.sharding import Mesh
from jax.sharding import PartitionSpec as P

WIDE = ("y", "z")
NARROW = ("x", "c")


def gather_rows(block, name):
    n = 1
    for axis in name:
        n *= lax.axis_size(axis)
    copies = jnp.broadcast_to(block[None], (n,) + block.shape)
    got = lax.all_to_all(copies, name, 0, 0, tiled=True)
    return got.reshape((n * block.shape[0],) + block.shape[1:])


def local(
    amplitudes, integrals, virtual_irrep, column_irrep, pair_energy, virtual_energy, residual_in
):
    nz = lax.axis_size("z")
    wide_size = lax.axis_size("y") * nz
    num_virt = virtual_irrep.shape[0]
    a_local = num_virt // wide_size
    wide_index = lax.axis_index("y") * nz + lax.axis_index("z")
    first_a = wide_index * a_local
    core = lax.axis_index("c")
    nx, nc = lax.axis_size("x"), lax.axis_size("c")
    swap = [(0, 1), (1, 0)]
    partner_integrals = lax.ppermute(integrals, "c", swap)
    partner_irrep = lax.ppermute(column_irrep, "c", swap)
    local_irrep = lax.dynamic_slice_in_dim(virtual_irrep, first_a, a_local, 0)
    row_irrep = jnp.bitwise_xor(local_irrep[:, None], virtual_irrep[None, :]).reshape(
        a_local * num_virt
    )
    zero = jnp.zeros((), integrals.dtype)
    masked = jnp.where(row_irrep[:, None] == column_irrep[None, :], integrals, zero)
    masked_partner = jnp.where(
        row_irrep[:, None] == partner_irrep[None, :], partner_integrals, zero
    )
    amp = gather_rows(amplitudes, WIDE)
    block = amp.shape[0] // (nx * nc)
    amp = amp.reshape(nx, nc, block, amp.shape[1])
    own = lax.dynamic_index_in_dim(amp, core, 1, keepdims=False)
    given = lax.dynamic_index_in_dim(amp, 1 - core, 1, keepdims=False)
    other = lax.ppermute(given, "c", swap)
    pairs = nx * block
    own = own.reshape(pairs, -1)
    other = other.reshape(pairs, -1)
    contract = (((1,), (1,)), ((), ()))
    part_own = lax.dot_general(own, masked, contract, preferred_element_type=jnp.float32)
    part_other = lax.dot_general(
        other, masked_partner, contract, preferred_element_type=jnp.float32
    )
    pair_sum = part_own.astype(jnp.bfloat16).astype(jnp.float32) + part_other.astype(
        jnp.bfloat16
    ).astype(jnp.float32)
    parts = pair_sum.astype(jnp.bfloat16).reshape(nx, block, pair_sum.shape[1])
    parts = lax.all_to_all(parts, "x", 0, 0, tiled=True)
    ladder = parts.astype(jnp.float32).sum(axis=0)
    pair_rows = ladder.shape[0]
    outgoing = ladder.astype(jnp.bfloat16).reshape(pair_rows, a_local, wide_size, a_local)
    outgoing = jnp.transpose(outgoing, (2, 0, 1, 3))
    got = lax.all_to_all(outgoing, WIDE, 0, 0, tiled=True)
    mirrored = jnp.transpose(got, (1, 3, 0, 2)).astype(jnp.float32)
    mirrored = mirrored.reshape(pair_rows, a_local * num_virt)
    local_energy = lax.dynamic_slice_in_dim(virtual_energy, first_a, a_local, 0)
    denominator = (
        pair_energy[:, None, None] - local_energy[None, :, None] - virtual_energy[None, None, :]
    )
    denominator = denominator.reshape(pair_rows, a_local * num_virt)
    total = residual_in.astype(jnp.float32) + ladder - mirrored
    return (total / denominator).astype(jnp.bfloat16)


def solution(mesh):
    wide, narrow = mesh.devices.shape
    fine = Mesh(mesh.devices.reshape(8, wide // 8, narrow // 2, 2), ("y", "z", "x", "c"))
    return jax.shard_map(
        local,
        mesh=fine,
        in_specs=(
            P(WIDE, NARROW),
            P(WIDE, NARROW),
            P(),
            P(NARROW),
            P(NARROW),
            P(),
            P(NARROW, WIDE),
        ),
        out_specs=P(NARROW, WIDE),
        check_vma=False,
    )
```

```python
import jax
import jax.numpy as jnp
from jax import lax
from jax.sharding import Mesh
from jax.sharding import PartitionSpec as P

WIDE = ("y", "z")
NARROW = ("x", "c")


def gather_rows(block, name):
    n = 1
    for axis in name:
        n *= lax.axis_size(axis)
    copies = jnp.broadcast_to(block[None], (n,) + block.shape)
    got = lax.all_to_all(copies, name, 0, 0, tiled=True)
    return got.reshape((n * block.shape[0],) + block.shape[1:])


def local(
    amplitudes, integrals, virtual_irrep, column_irrep, pair_energy, virtual_energy, residual_in
):
    nz = lax.axis_size("z")
    wide_size = lax.axis_size("y") * nz
    num_virt = virtual_irrep.shape[0]
    a_local = num_virt // wide_size
    wide_index = lax.axis_index("y") * nz + lax.axis_index("z")
    first_a = wide_index * a_local
    core = lax.axis_index("c")
    nx, nc = lax.axis_size("x"), lax.axis_size("c")
    swap = [(0, 1), (1, 0)]
    partner_integrals = lax.ppermute(integrals, "c", swap)
    local_irrep = lax.dynamic_slice_in_dim(virtual_irrep, first_a, a_local, 0)
    row_irrep = jnp.bitwise_xor(local_irrep[:, None], virtual_irrep[None, :]).reshape(
        a_local * num_virt
    )
    zero = jnp.zeros((), integrals.dtype)
    masked = jnp.where(row_irrep[:, None] == column_irrep[None, :], integrals, zero)
    amp = gather_rows(amplitudes, WIDE)
    block = amp.shape[0] // (nx * nc)
    amp = amp.reshape(nx, nc, block, amp.shape[1])
    own = lax.dynamic_index_in_dim(amp, core, 1, keepdims=False)
    given = lax.dynamic_index_in_dim(amp, 1 - core, 1, keepdims=False)
    pairs = nx * block
    labels = column_irrep.astype(amp.dtype)[None, :]
    sent = jnp.concatenate([given.reshape(pairs, -1), labels], axis=0)
    sent = lax.ppermute(sent, "c", swap)
    other = sent[:pairs]
    partner_irrep = sent[pairs].astype(column_irrep.dtype)
    own = own.reshape(pairs, -1)
    masked_partner = jnp.where(
        row_irrep[:, None] == partner_irrep[None, :], partner_integrals, zero
    )
    contract = (((1,), (1,)), ((), ()))
    part_own = lax.dot_general(own, masked, contract, preferred_element_type=jnp.float32)
    part_other = lax.dot_general(
        other, masked_partner, contract, preferred_element_type=jnp.float32
    )
    pair_sum = part_own.astype(jnp.bfloat16).astype(jnp.float32) + part_other.astype(
        jnp.bfloat16
    ).astype(jnp.float32)
    parts = pair_sum.astype(jnp.bfloat16).reshape(nx, block, pair_sum.shape[1])
    parts = lax.all_to_all(parts, "x", 0, 0, tiled=True)
    ladder = parts.astype(jnp.float32).sum(axis=0)
    pair_rows = ladder.shape[0]
    outgoing = ladder.astype(jnp.bfloat16).reshape(pair_rows, a_local, wide_size, a_local)
    outgoing = jnp.transpose(outgoing, (2, 0, 1, 3))
    got = lax.all_to_all(outgoing, WIDE, 0, 0, tiled=True)
    mirrored = jnp.transpose(got, (1, 3, 0, 2)).astype(jnp.float32)
    mirrored = mirrored.reshape(pair_rows, a_local * num_virt)
    local_energy = lax.dynamic_slice_in_dim(virtual_energy, first_a, a_local, 0)
    denominator = (
        pair_energy[:, None, None] - local_energy[None, :, None] - virtual_energy[None, None, :]
    )
    denominator = denominator.reshape(pair_rows, a_local * num_virt)
    total = residual_in.astype(jnp.float32) + ladder - mirrored
    return (total / denominator).astype(jnp.bfloat16)


def solution(mesh):
    wide, narrow = mesh.devices.shape
    fine = Mesh(mesh.devices.reshape(8, wide // 8, narrow // 2, 2), ("y", "z", "x", "c"))
    return jax.shard_map(
        local,
        mesh=fine,
        in_specs=(
            P(WIDE, NARROW),
            P(WIDE, NARROW),
            P(),
            P(NARROW),
            P(NARROW),
            P(),
            P(NARROW, WIDE),
        ),
        out_specs=P(NARROW, WIDE),
        check_vma=False,
    )
```

```python
import jax
import jax.numpy as jnp
from jax import lax
from jax.sharding import Mesh
from jax.sharding import PartitionSpec as P

WIDE = ("y", "z")
NARROW = ("x", "c")


def gather_rows(block, name):
    n = 1
    for axis in name:
        n *= lax.axis_size(axis)
    copies = jnp.broadcast_to(block[None], (n,) + block.shape)
    got = lax.all_to_all(copies, name, 0, 0, tiled=True)
    return got.reshape((n * block.shape[0],) + block.shape[1:])


def local(
    amplitudes, integrals, virtual_irrep, column_irrep, pair_energy, virtual_energy, residual_in
):
    nz = lax.axis_size("z")
    wide_size = lax.axis_size("y") * nz
    num_virt = virtual_irrep.shape[0]
    a_local = num_virt // wide_size
    wide_index = lax.axis_index("y") * nz + lax.axis_index("z")
    first_a = wide_index * a_local
    core = lax.axis_index("c")
    nx, nc = lax.axis_size("x"), lax.axis_size("c")
    swap = [(0, 1), (1, 0)]
    partner_integrals = lax.ppermute(integrals, "c", swap)
    local_irrep = lax.dynamic_slice_in_dim(virtual_irrep, first_a, a_local, 0)
    row_irrep = jnp.bitwise_xor(local_irrep[:, None], virtual_irrep[None, :]).reshape(
        a_local * num_virt
    )
    zero = jnp.zeros((), integrals.dtype)
    masked = jnp.where(row_irrep[:, None] == column_irrep[None, :], integrals, zero)
    amp = gather_rows(amplitudes, WIDE)
    block = amp.shape[0] // (nx * nc)
    amp = amp.reshape(nx, nc, block, amp.shape[1])
    own = lax.dynamic_index_in_dim(amp, core, 1, keepdims=False)
    given = lax.dynamic_index_in_dim(amp, 1 - core, 1, keepdims=False)
    pairs = nx * block
    labels = column_irrep.astype(amp.dtype)[None, :]
    sent = jnp.concatenate([given.reshape(pairs, -1), labels], axis=0)
    sent = lax.ppermute(sent, "c", swap)
    other = sent[:pairs]
    partner_irrep = sent[pairs].astype(column_irrep.dtype)
    own = own.reshape(pairs, -1)
    masked_partner = jnp.where(
        row_irrep[:, None] == partner_irrep[None, :], partner_integrals, zero
    )
    contract = (((1,), (1,)), ((), ()))
    part_own = lax.dot_general(own, masked, contract, preferred_element_type=jnp.float32)
    part_other = lax.dot_general(
        other, masked_partner, contract, preferred_element_type=jnp.float32
    )
    pair_sum = part_own.astype(jnp.bfloat16).astype(jnp.float32) + part_other.astype(
        jnp.bfloat16
    ).astype(jnp.float32)
    parts = pair_sum.astype(jnp.bfloat16).reshape(nx, block, pair_sum.shape[1])
    parts = lax.all_to_all(parts, "x", 0, 0, tiled=True)
    ladder = parts.astype(jnp.float32).sum(axis=0)
    pair_rows = ladder.shape[0]
    outgoing = ladder.astype(jnp.bfloat16).reshape(pair_rows, a_local, wide_size, a_local)
    outgoing = jnp.transpose(outgoing, (2, 0, 1, 3))
    got = lax.all_to_all(outgoing, WIDE, 0, 0, tiled=True)
    partial = residual_in.astype(jnp.float32) + ladder
    partial, got = lax.optimization_barrier((partial, got))
    mirrored = jnp.transpose(got, (1, 3, 0, 2)).astype(jnp.float32)
    mirrored = mirrored.reshape(pair_rows, a_local * num_virt)
    local_energy = lax.dynamic_slice_in_dim(virtual_energy, first_a, a_local, 0)
    denominator = (
        pair_energy[:, None, None] - local_energy[None, :, None] - virtual_energy[None, None, :]
    )
    denominator = denominator.reshape(pair_rows, a_local * num_virt)
    total = partial - mirrored
    return (total / denominator).astype(jnp.bfloat16)


def solution(mesh):
    wide, narrow = mesh.devices.shape
    fine = Mesh(mesh.devices.reshape(8, wide // 8, narrow // 2, 2), ("y", "z", "x", "c"))
    return jax.shard_map(
        local,
        mesh=fine,
        in_specs=(
            P(WIDE, NARROW),
            P(WIDE, NARROW),
            P(),
            P(NARROW),
            P(NARROW),
            P(),
            P(NARROW, WIDE),
        ),
        out_specs=P(NARROW, WIDE),
        check_vma=False,
    )
```

```python
import jax
import jax.numpy as jnp
from jax import lax
from jax.experimental import pallas as pl
from jax.experimental.pallas import tpu as pltpu
from jax.sharding import Mesh
from jax.sharding import PartitionSpec as P

WIDE = ("y", "z")
NARROW = ("x", "c")


def gather_rows(block, name):
    n = 1
    for axis in name:
        n *= lax.axis_size(axis)
    copies = jnp.broadcast_to(block[None], (n,) + block.shape)
    got = lax.all_to_all(copies, name, 0, 0, tiled=True)
    return got.reshape((n * block.shape[0],) + block.shape[1:])


def pair_ladder(own, other, integrals, partner_integrals, local_irrep, virtual_irrep, labels, partner_labels):
    pairs, cd_local = own.shape
    a_local = local_irrep.shape[0]
    num_virt = virtual_irrep.shape[0]

    def kernel(li_ref, own_ref, other_ref, v_ref, vp_ref, vi_ref, col_ref, colp_ref, out_ref):
        pair_irrep = jnp.bitwise_xor(vi_ref[...], li_ref[pl.program_id(0)])
        zero = jnp.zeros((), v_ref.dtype)
        v = jnp.where(pair_irrep == col_ref[...], v_ref[...], zero)
        vp = jnp.where(pair_irrep == colp_ref[...], vp_ref[...], zero)
        contract = (((1,), (1,)), ((), ()))
        p1 = lax.dot_general(own_ref[...], v, contract, preferred_element_type=jnp.float32)
        p2 = lax.dot_general(other_ref[...], vp, contract, preferred_element_type=jnp.float32)
        total = p1.astype(jnp.bfloat16).astype(jnp.float32) + p2.astype(jnp.bfloat16).astype(
            jnp.float32
        )
        out_ref[...] = total.astype(out_ref.dtype)

    whole = lambda a, li: (0, 0)
    rows = lambda a, li: (a, 0)
    grid_spec = pltpu.PrefetchScalarGridSpec(
        num_scalar_prefetch=1,
        grid=(a_local,),
        in_specs=[
            pl.BlockSpec((pairs, cd_local), whole),
            pl.BlockSpec((pairs, cd_local), whole),
            pl.BlockSpec((num_virt, cd_local), rows),
            pl.BlockSpec((num_virt, cd_local), rows),
            pl.BlockSpec((num_virt, 1), whole),
            pl.BlockSpec((1, cd_local), whole),
            pl.BlockSpec((1, cd_local), whole),
        ],
        out_specs=pl.BlockSpec((pairs, num_virt), lambda a, li: (0, a)),
    )
    return pl.pallas_call(
        kernel,
        grid_spec=grid_spec,
        out_shape=jax.ShapeDtypeStruct((pairs, a_local * num_virt), jnp.bfloat16),
    )(
        local_irrep,
        own,
        other,
        integrals,
        partner_integrals,
        virtual_irrep.reshape(num_virt, 1),
        labels.reshape(1, cd_local),
        partner_labels.reshape(1, cd_local),
    )


def local(
    amplitudes, integrals, virtual_irrep, column_irrep, pair_energy, virtual_energy, residual_in
):
    nz = lax.axis_size("z")
    wide_size = lax.axis_size("y") * nz
    num_virt = virtual_irrep.shape[0]
    a_local = num_virt // wide_size
    wide_index = lax.axis_index("y") * nz + lax.axis_index("z")
    first_a = wide_index * a_local
    core = lax.axis_index("c")
    nx, nc = lax.axis_size("x"), lax.axis_size("c")
    swap = [(0, 1), (1, 0)]
    partner_integrals = lax.ppermute(integrals, "c", swap)
    local_irrep = lax.dynamic_slice_in_dim(virtual_irrep, first_a, a_local, 0)
    amp = gather_rows(amplitudes, WIDE)
    block = amp.shape[0] // (nx * nc)
    amp = amp.reshape(nx, nc, block, amp.shape[1])
    own = lax.dynamic_index_in_dim(amp, core, 1, keepdims=False)
    given = lax.dynamic_index_in_dim(amp, 1 - core, 1, keepdims=False)
    pairs = nx * block
    labels = column_irrep.astype(amp.dtype)[None, :]
    sent = jnp.concatenate([given.reshape(pairs, -1), labels], axis=0)
    sent = lax.ppermute(sent, "c", swap)
    other = sent[:pairs]
    partner_irrep = sent[pairs].astype(column_irrep.dtype)
    own = own.reshape(pairs, -1)
    pair_sum = pair_ladder(
        own, other, integrals, partner_integrals, local_irrep, virtual_irrep,
        column_irrep, partner_irrep,
    )
    parts = pair_sum.reshape(nx, block, pair_sum.shape[1])
    parts = lax.all_to_all(parts, "x", 0, 0, tiled=True)
    ladder = parts.astype(jnp.float32).sum(axis=0)
    pair_rows = ladder.shape[0]
    outgoing = ladder.astype(jnp.bfloat16).reshape(pair_rows, a_local, wide_size, a_local)
    outgoing = jnp.transpose(outgoing, (2, 0, 1, 3))
    got = lax.all_to_all(outgoing, WIDE, 0, 0, tiled=True)
    mirrored = jnp.transpose(got, (1, 3, 0, 2)).astype(jnp.float32)
    mirrored = mirrored.reshape(pair_rows, a_local * num_virt)
    local_energy = lax.dynamic_slice_in_dim(virtual_energy, first_a, a_local, 0)
    denominator = (
        pair_energy[:, None, None] - local_energy[None, :, None] - virtual_energy[None, None, :]
    )
    denominator = denominator.reshape(pair_rows, a_local * num_virt)
    total = residual_in.astype(jnp.float32) + ladder - mirrored
    return (total / denominator).astype(jnp.bfloat16)


def solution(mesh):
    wide, narrow = mesh.devices.shape
    fine = Mesh(mesh.devices.reshape(8, wide // 8, narrow // 2, 2), ("y", "z", "x", "c"))
    return jax.shard_map(
        local,
        mesh=fine,
        in_specs=(
            P(WIDE, NARROW),
            P(WIDE, NARROW),
            P(),
            P(NARROW),
            P(NARROW),
            P(),
            P(NARROW, WIDE),
        ),
        out_specs=P(NARROW, WIDE),
        check_vma=False,
    )
```

```python
import jax
import jax.numpy as jnp
from jax import lax
from jax.sharding import Mesh
from jax.sharding import PartitionSpec as P

WIDE = ("y", "z")
NARROW = ("x", "c")


def gather_rows(block, name):
    n = 1
    for axis in name:
        n *= lax.axis_size(axis)
    copies = jnp.broadcast_to(block[None], (n,) + block.shape)
    got = lax.all_to_all(copies, name, 0, 0, tiled=True)
    return got.reshape((n * block.shape[0],) + block.shape[1:])


def local(
    amplitudes, integrals, virtual_irrep, column_irrep, pair_energy, virtual_energy, residual_in
):
    nz = lax.axis_size("z")
    wide_size = lax.axis_size("y") * nz
    num_virt = virtual_irrep.shape[0]
    a_local = num_virt // wide_size
    wide_index = lax.axis_index("y") * nz + lax.axis_index("z")
    first_a = wide_index * a_local
    core = lax.axis_index("c")
    nx, nc = lax.axis_size("x"), lax.axis_size("c")
    swap = [(0, 1), (1, 0)]
    partner_integrals = lax.ppermute(integrals, "c", swap)
    local_irrep = lax.dynamic_slice_in_dim(virtual_irrep, first_a, a_local, 0)
    row_irrep = jnp.bitwise_xor(local_irrep[:, None], virtual_irrep[None, :]).reshape(
        a_local * num_virt
    )
    zero = jnp.zeros((), integrals.dtype)
    masked = jnp.where(row_irrep[:, None] == column_irrep[None, :], integrals, zero)
    amp = gather_rows(amplitudes, WIDE)
    block = amp.shape[0] // (nx * nc)
    amp = amp.reshape(nx, nc, block, amp.shape[1])
    own = lax.dynamic_index_in_dim(amp, core, 1, keepdims=False)
    given = lax.dynamic_index_in_dim(amp, 1 - core, 1, keepdims=False)
    pairs = nx * block
    labels = column_irrep.astype(amp.dtype)[None, :]
    sent = jnp.concatenate([given.reshape(pairs, -1), labels], axis=0)
    sent = lax.ppermute(sent, "c", swap)
    other = sent[:pairs]
    partner_irrep = sent[pairs].astype(column_irrep.dtype)
    own = own.reshape(pairs, -1)
    masked_partner = jnp.where(
        row_irrep[:, None] == partner_irrep[None, :], partner_integrals, zero
    )
    contract = (((1,), (1,)), ((), ()))
    part_own = lax.dot_general(own, masked, contract, preferred_element_type=jnp.float32)
    part_other = lax.dot_general(
        other, masked_partner, contract, preferred_element_type=jnp.float32
    )
    pair_sum = part_own.astype(jnp.bfloat16).astype(jnp.float32) + part_other.astype(
        jnp.bfloat16
    ).astype(jnp.float32)
    parts = pair_sum.astype(jnp.bfloat16).reshape(nx, block, pair_sum.shape[1])
    here = lax.axis_index("x")
    ladder = lax.dynamic_index_in_dim(parts, here, 0, keepdims=False).astype(jnp.float32)
    for step in range(1, nx):
        outgoing_block = lax.dynamic_index_in_dim(parts, (here + step) % nx, 0, keepdims=False)
        pairs_step = [(i, (i + step) % nx) for i in range(nx)]
        ladder = ladder + lax.ppermute(outgoing_block, "x", pairs_step).astype(jnp.float32)
    pair_rows = ladder.shape[0]
    outgoing = ladder.astype(jnp.bfloat16).reshape(pair_rows, a_local, wide_size, a_local)
    outgoing = jnp.transpose(outgoing, (2, 0, 1, 3))
    got = lax.all_to_all(outgoing, WIDE, 0, 0, tiled=True)
    mirrored = jnp.transpose(got, (1, 3, 0, 2)).astype(jnp.float32)
    mirrored = mirrored.reshape(pair_rows, a_local * num_virt)
    local_energy = lax.dynamic_slice_in_dim(virtual_energy, first_a, a_local, 0)
    denominator = (
        pair_energy[:, None, None] - local_energy[None, :, None] - virtual_energy[None, None, :]
    )
    denominator = denominator.reshape(pair_rows, a_local * num_virt)
    total = residual_in.astype(jnp.float32) + ladder - mirrored
    return (total / denominator).astype(jnp.bfloat16)


def solution(mesh):
    wide, narrow = mesh.devices.shape
    fine = Mesh(mesh.devices.reshape(8, wide // 8, narrow // 2, 2), ("y", "z", "x", "c"))
    return jax.shard_map(
        local,
        mesh=fine,
        in_specs=(
            P(WIDE, NARROW),
            P(WIDE, NARROW),
            P(),
            P(NARROW),
            P(NARROW),
            P(),
            P(NARROW, WIDE),
        ),
        out_specs=P(NARROW, WIDE),
        check_vma=False,
    )
```

```python
import jax
import jax.numpy as jnp
from jax import lax
from jax.sharding import Mesh
from jax.sharding import PartitionSpec as P

WIDE = ("y", "z")
NARROW = ("x", "c")


def gather_rows(block, name):
    n = 1
    for axis in name:
        n *= lax.axis_size(axis)
    copies = jnp.broadcast_to(block[None], (n,) + block.shape)
    got = lax.all_to_all(copies, name, 0, 0, tiled=True)
    return got.reshape((n * block.shape[0],) + block.shape[1:])


def local(
    amplitudes, integrals, virtual_irrep, column_irrep, pair_energy, virtual_energy, residual_in
):
    nz = lax.axis_size("z")
    wide_size = lax.axis_size("y") * nz
    num_virt = virtual_irrep.shape[0]
    a_local = num_virt // wide_size
    wide_index = lax.axis_index("y") * nz + lax.axis_index("z")
    first_a = wide_index * a_local
    core = lax.axis_index("c")
    nx, nc = lax.axis_size("x"), lax.axis_size("c")
    swap = [(0, 1), (1, 0)]
    partner_integrals = lax.ppermute(integrals, "c", swap)
    local_irrep = lax.dynamic_slice_in_dim(virtual_irrep, first_a, a_local, 0)
    row_irrep = jnp.bitwise_xor(local_irrep[:, None], virtual_irrep[None, :]).reshape(
        a_local * num_virt
    )
    zero = jnp.zeros((), integrals.dtype)
    masked = jnp.where(row_irrep[:, None] == column_irrep[None, :], integrals, zero)
    amp = gather_rows(amplitudes, WIDE)
    block = amp.shape[0] // (nx * nc)
    amp = amp.reshape(nx, nc, block, amp.shape[1])
    own = lax.dynamic_index_in_dim(amp, core, 1, keepdims=False)
    given = lax.dynamic_index_in_dim(amp, 1 - core, 1, keepdims=False)
    pairs = nx * block
    labels = column_irrep.astype(amp.dtype)[None, :]
    sent = jnp.concatenate([given.reshape(pairs, -1), labels], axis=0)
    sent = lax.ppermute(sent, "c", swap)
    other = sent[:pairs]
    partner_irrep = sent[pairs].astype(column_irrep.dtype)
    own = own.reshape(pairs, -1)
    masked_partner = jnp.where(
        row_irrep[:, None] == partner_irrep[None, :], partner_integrals, zero
    )
    contract = (((1,), (1,)), ((), ()))
    part_own = lax.dot_general(own, masked, contract, preferred_element_type=jnp.float32)
    part_other = lax.dot_general(
        other, masked_partner, contract, preferred_element_type=jnp.float32
    )
    pair_sum = part_own.astype(jnp.bfloat16).astype(jnp.float32) + part_other.astype(
        jnp.bfloat16
    ).astype(jnp.float32)
    parts = pair_sum.astype(jnp.bfloat16).reshape(nx, block, pair_sum.shape[1])
    parts = lax.all_to_all(parts, "x", 0, 0, tiled=True)
    ladder = parts.astype(jnp.float32).sum(axis=0)
    pair_rows = ladder.shape[0]
    outgoing = ladder.astype(jnp.bfloat16).reshape(pair_rows, a_local, wide_size, a_local)
    outgoing = jnp.transpose(outgoing, (2, 0, 1, 3))
    got = lax.all_to_all(outgoing, WIDE, 0, 0, tiled=True)
    mirrored = jnp.transpose(got, (1, 3, 0, 2)).reshape(pair_rows, a_local * num_virt)
    mirrored = lax.optimization_barrier(mirrored).astype(jnp.float32)
    local_energy = lax.dynamic_slice_in_dim(virtual_energy, first_a, a_local, 0)
    denominator = (
        pair_energy[:, None, None] - local_energy[None, :, None] - virtual_energy[None, None, :]
    )
    denominator = denominator.reshape(pair_rows, a_local * num_virt)
    total = residual_in.astype(jnp.float32) + ladder - mirrored
    return (total / denominator).astype(jnp.bfloat16)


def solution(mesh):
    wide, narrow = mesh.devices.shape
    fine = Mesh(mesh.devices.reshape(8, wide // 8, narrow // 2, 2), ("y", "z", "x", "c"))
    return jax.shard_map(
        local,
        mesh=fine,
        in_specs=(
            P(WIDE, NARROW),
            P(WIDE, NARROW),
            P(),
            P(NARROW),
            P(NARROW),
            P(),
            P(NARROW, WIDE),
        ),
        out_specs=P(NARROW, WIDE),
        check_vma=False,
    )
```

```python
import jax
import jax.numpy as jnp
from jax import lax
from jax.sharding import Mesh
from jax.sharding import PartitionSpec as P

WIDE = ("y", "z")
NARROW = ("x", "c")


def gather_rows(block, name):
    n = 1
    for axis in name:
        n *= lax.axis_size(axis)
    copies = jnp.broadcast_to(block[None], (n,) + block.shape)
    got = lax.all_to_all(copies, name, 0, 0, tiled=True)
    return got.reshape((n * block.shape[0],) + block.shape[1:])


def local(
    amplitudes, integrals, virtual_irrep, column_irrep, pair_energy, virtual_energy, residual_in
):
    nz = lax.axis_size("z")
    wide_size = lax.axis_size("y") * nz
    num_virt = virtual_irrep.shape[0]
    a_local = num_virt // wide_size
    wide_index = lax.axis_index("y") * nz + lax.axis_index("z")
    first_a = wide_index * a_local
    core = lax.axis_index("c")
    nx, nc = lax.axis_size("x"), lax.axis_size("c")
    swap = [(0, 1), (1, 0)]
    partner_integrals = lax.ppermute(integrals, "c", swap)
    local_irrep = lax.dynamic_slice_in_dim(virtual_irrep, first_a, a_local, 0)
    row_irrep = jnp.bitwise_xor(local_irrep[:, None], virtual_irrep[None, :]).reshape(
        a_local * num_virt
    )
    zero = jnp.zeros((), integrals.dtype)
    masked = jnp.where(row_irrep[:, None] == column_irrep[None, :], integrals, zero)
    amp = gather_rows(amplitudes, WIDE)
    block = amp.shape[0] // (nx * nc)
    amp = amp.reshape(nx, nc, block, amp.shape[1])
    own = lax.dynamic_index_in_dim(amp, core, 1, keepdims=False)
    given = lax.dynamic_index_in_dim(amp, 1 - core, 1, keepdims=False)
    pairs = nx * block
    labels = column_irrep.astype(amp.dtype)[None, :]
    sent = jnp.concatenate([given.reshape(pairs, -1), labels], axis=0)
    sent = lax.ppermute(sent, "c", swap)
    other = sent[:pairs]
    partner_irrep = sent[pairs].astype(column_irrep.dtype)
    own = own.reshape(pairs, -1)
    masked_partner = jnp.where(
        row_irrep[:, None] == partner_irrep[None, :], partner_integrals, zero
    )
    contract = (((1,), (1,)), ((), ()))
    part_own = lax.dot_general(own, masked, contract, preferred_element_type=jnp.float32)
    part_other = lax.dot_general(
        other, masked_partner, contract, preferred_element_type=jnp.float32
    )
    pair_sum = part_own.astype(jnp.bfloat16).astype(jnp.float32) + part_other.astype(
        jnp.bfloat16
    ).astype(jnp.float32)
    parts = pair_sum.astype(jnp.bfloat16).reshape(nx, block, pair_sum.shape[1])
    parts = lax.all_to_all(parts, "x", 0, 0, tiled=True)
    ladder = parts.astype(jnp.float32).sum(axis=0)
    pair_rows = ladder.shape[0]
    outgoing = ladder.astype(jnp.bfloat16).reshape(pair_rows, a_local, wide_size, a_local)
    outgoing = jnp.transpose(outgoing, (2, 0, 1, 3)).reshape(wide_size, 2, -1)
    outgoing = lax.optimization_barrier(outgoing)
    got = lax.all_to_all(outgoing, WIDE, 0, 0, tiled=True)
    got = got.reshape(wide_size, pair_rows, a_local, a_local)
    mirrored = jnp.transpose(got, (1, 3, 0, 2)).reshape(pair_rows, a_local * num_virt)
    mirrored = lax.optimization_barrier(mirrored).astype(jnp.float32)
    local_energy = lax.dynamic_slice_in_dim(virtual_energy, first_a, a_local, 0)
    denominator = (
        pair_energy[:, None, None] - local_energy[None, :, None] - virtual_energy[None, None, :]
    )
    denominator = denominator.reshape(pair_rows, a_local * num_virt)
    total = residual_in.astype(jnp.float32) + ladder - mirrored
    return (total / denominator).astype(jnp.bfloat16)


def solution(mesh):
    wide, narrow = mesh.devices.shape
    fine = Mesh(mesh.devices.reshape(8, wide // 8, narrow // 2, 2), ("y", "z", "x", "c"))
    return jax.shard_map(
        local,
        mesh=fine,
        in_specs=(
            P(WIDE, NARROW),
            P(WIDE, NARROW),
            P(),
            P(NARROW),
            P(NARROW),
            P(),
            P(NARROW, WIDE),
        ),
        out_specs=P(NARROW, WIDE),
        check_vma=False,
    )
```

```python
import jax
import jax.numpy as jnp
from jax import lax
from jax.sharding import Mesh
from jax.sharding import PartitionSpec as P

WIDE = ("y", "z")
NARROW = ("x", "c")


def gather_rows(block, name):
    n = 1
    for axis in name:
        n *= lax.axis_size(axis)
    copies = jnp.broadcast_to(block[None], (n,) + block.shape)
    got = lax.all_to_all(copies, name, 0, 0, tiled=True)
    return got.reshape((n * block.shape[0],) + block.shape[1:])


def local(
    amplitudes, integrals, virtual_irrep, column_irrep, pair_energy, virtual_energy, residual_in
):
    nz = lax.axis_size("z")
    wide_size = lax.axis_size("y") * nz
    num_virt = virtual_irrep.shape[0]
    a_local = num_virt // wide_size
    wide_index = lax.axis_index("y") * nz + lax.axis_index("z")
    first_a = wide_index * a_local
    core = lax.axis_index("c")
    nx, nc = lax.axis_size("x"), lax.axis_size("c")
    swap = [(0, 1), (1, 0)]
    partner_integrals = lax.ppermute(integrals, "c", swap)
    local_irrep = lax.dynamic_slice_in_dim(virtual_irrep, first_a, a_local, 0)
    row_irrep = jnp.bitwise_xor(local_irrep[:, None], virtual_irrep[None, :]).reshape(
        a_local * num_virt
    )
    zero = jnp.zeros((), integrals.dtype)
    masked = jnp.where(row_irrep[:, None] == column_irrep[None, :], integrals, zero)
    amp = gather_rows(amplitudes, WIDE)
    block = amp.shape[0] // (nx * nc)
    amp = amp.reshape(nx, nc, block, amp.shape[1])
    own = lax.dynamic_index_in_dim(amp, core, 1, keepdims=False)
    given = lax.dynamic_index_in_dim(amp, 1 - core, 1, keepdims=False)
    pairs = nx * block
    labels = column_irrep.astype(amp.dtype)[None, :]
    sent = jnp.concatenate([given.reshape(pairs, -1), labels], axis=0)
    sent = lax.ppermute(sent, "c", swap)
    other = sent[:pairs]
    partner_irrep = sent[pairs].astype(column_irrep.dtype)
    own = own.reshape(pairs, -1)
    masked_partner = jnp.where(
        row_irrep[:, None] == partner_irrep[None, :], partner_integrals, zero
    )
    contract = (((1,), (1,)), ((), ()))
    part_own = lax.dot_general(own, masked, contract, preferred_element_type=jnp.float32)
    part_other = lax.dot_general(
        other, masked_partner, contract, preferred_element_type=jnp.float32
    )
    part_own = lax.optimization_barrier(part_own.astype(jnp.bfloat16))
    pair_sum = part_own.astype(jnp.float32) + part_other.astype(jnp.bfloat16).astype(jnp.float32)
    parts = pair_sum.astype(jnp.bfloat16).reshape(nx, block, pair_sum.shape[1])
    parts = lax.all_to_all(parts, "x", 0, 0, tiled=True)
    ladder = parts.astype(jnp.float32).sum(axis=0)
    pair_rows = ladder.shape[0]
    outgoing = ladder.astype(jnp.bfloat16).reshape(pair_rows, a_local, wide_size, a_local)
    outgoing = jnp.transpose(outgoing, (2, 0, 1, 3))
    got = lax.all_to_all(outgoing, WIDE, 0, 0, tiled=True)
    mirrored = jnp.transpose(got, (1, 3, 0, 2)).reshape(pair_rows, a_local * num_virt)
    mirrored = lax.optimization_barrier(mirrored).astype(jnp.float32)
    local_energy = lax.dynamic_slice_in_dim(virtual_energy, first_a, a_local, 0)
    denominator = (
        pair_energy[:, None, None] - local_energy[None, :, None] - virtual_energy[None, None, :]
    )
    denominator = denominator.reshape(pair_rows, a_local * num_virt)
    total = residual_in.astype(jnp.float32) + ladder - mirrored
    return (total / denominator).astype(jnp.bfloat16)


def solution(mesh):
    wide, narrow = mesh.devices.shape
    fine = Mesh(mesh.devices.reshape(8, wide // 8, narrow // 2, 2), ("y", "z", "x", "c"))
    return jax.shard_map(
        local,
        mesh=fine,
        in_specs=(
            P(WIDE, NARROW),
            P(WIDE, NARROW),
            P(),
            P(NARROW),
            P(NARROW),
            P(),
            P(NARROW, WIDE),
        ),
        out_specs=P(NARROW, WIDE),
        check_vma=False,
    )
```
